256 devices in a mesh: rep: 8 (over x, core), seq: 32 (over y, z).
Axes of the slice: x: 4, y: 4, z: 8, core: 2. Of those that a mesh axis runs over, the one named last changes fastest.
Arguments:
- tokens: bfloat16 [16, 256, 32, 1024], P('rep', 'seq'), may hold values from -250 to 250
- cotangent: bfloat16 [16, 256, 32, 1024], P('rep', 'seq'), may hold values from -6 to 6
- clip_counts: int32 [8], P('rep'), may hold values from 1 to 2, as said below
- windows: int32 [16, 4, 3], P('rep'), may hold values from 0 to 3, as said below
- window_counts: int32 [16, 4], P('rep'), may hold values from 1 to 3, as said below
- norm_gain: float32 [1024], replicated, may hold values from 0.5 to 4
- norm_bias: float32 [1024], replicated, may hold values from -3 to 3
- qkv_weight: bfloat16 [1024, 3072], replicated, may hold values from -0.5 to 0.5
- out_weight: bfloat16 [1024, 1024], replicated, may hold values from -0.1875 to 0.1875
Outputs:
- grad_input: bfloat16 [16, 256, 32, 1024], P('rep', 'seq')
- grad_qkv_weight: float32 [1024, 3072], P('seq')
- grad_out_weight: float32 [1024, 1024], P('seq')
- grad_gain: float32 [1024], P('seq')
- grad_bias: float32 [1024], P('seq')
The draws below stay inside these ranges and needn't reach their ends.
Inputs may be any that keep to these rules, and one draw needn't show every extreme that they name: `clip_counts`: slots of a group at or past its count hold no clip; some group is full. `windows`: the first entry of each list is the window itself; the entries of a list are distinct. `window_counts`: some window of every clip uses all 3 entries.
All inputs are finite; a program needn't handle non-finite values.
Results may differ from the reference program's by a relative error of at most 0.025.
The reference program's roundings to bfloat16 on the way count: a program that leaves them out, or rounds other values in their place, can miss the bound.
Values may be sent and summed in bfloat16 or wider, within the bound.
No kernel may reach another device: no remote copies, remote signals or barrier semaphores. Data moves between devices by JAX's collectives and lax.ppermute only.
A program may use at most 128 MiB of HBM per device.

```python
import math
import jax
import jax.numpy as jnp
from jax import lax

D = 1024
HEADS = 16
HEAD_DIM = 64
P_SIZE = 32
F = 256
WIN = 64
MAXW = 3
CLIPS = 2
NWIN = 4
GROUPS = 8
CLIPS_ALL = 16
TOKENS = 131072


def draw_tokens(key, part):
    shape_all = (CLIPS_ALL, F, P_SIZE, D)
    row_scale = jnp.exp(jax.random.uniform(jax.random.fold_in(key, 1), (CLIPS_ALL, F, P_SIZE, 1)) * math.log(10.0))
    col_scale = jnp.exp(jax.random.uniform(jax.random.fold_in(key, 2), (D,)) * math.log(4.0))
    base_draw = jax.random.truncated_normal(jax.random.fold_in(key, 3), -5.0, 5.0, shape_all)
    return (base_draw * row_scale * col_scale).astype(jnp.bfloat16)


def draw_qkv_weight(key, part):
    fan_scale = 1.0 / math.sqrt(D)
    query_part = jax.random.truncated_normal(jax.random.fold_in(key, 1), -5.0, 5.0, (D, D)) * fan_scale
    key_part = jax.random.truncated_normal(jax.random.fold_in(key, 2), -5.0, 5.0, (D, D)) * fan_scale
    value_part = jax.random.truncated_normal(jax.random.fold_in(key, 4), -5.0, 5.0, (D, D)) * fan_scale
    return jnp.concatenate([query_part, key_part, value_part], axis=1).astype(jnp.bfloat16)


def draw_norm_gain(key, part):
    gain_draw = jax.random.uniform(key, (D,), minval=0.6, maxval=1.6)
    return gain_draw.astype(jnp.float32)


def draw_clip_counts(key, part):
    drawn = jax.random.randint(key, (GROUPS,), 1, CLIPS + 1)
    chosen = jax.random.randint(jax.random.fold_in(key, 1), (), 0, GROUPS)
    return jnp.where(jnp.arange(GROUPS) == chosen, CLIPS, drawn).astype(jnp.int32)


def draw_windows(key, part):
    own_window = jnp.arange(NWIN)
    ranks = jax.random.randint(key, (CLIPS_ALL, NWIN, NWIN - 1), 0, 1 << 20) * (NWIN - 1) + jnp.arange(NWIN - 1)
    ordering = jnp.argsort(ranks, axis=-1)
    others = (own_window[None, :, None] + 1 + ordering) % NWIN
    first_entry = jnp.broadcast_to(own_window[None, :, None], (CLIPS_ALL, NWIN, 1))
    return jnp.concatenate([first_entry, others[:, :, :MAXW - 1]], axis=-1).astype(jnp.int32)


def draw_window_counts(key, part):
    drawn = jax.random.randint(key, (CLIPS_ALL, NWIN), 1, MAXW + 1)
    chosen = jax.random.randint(jax.random.fold_in(key, 1), (CLIPS_ALL,), 0, NWIN)
    return jnp.where(jnp.arange(NWIN)[None, :] == chosen[:, None], MAXW, drawn).astype(jnp.int32)


def levels(rng, dims, cuts, least, largest):
    factor_of, own = 1.0, jax.random.fold_in(rng, 6)
    for axis_at, shards_of in cuts:
        steps = jnp.exp(jax.random.uniform(jax.random.fold_in(own, axis_at), (shards_of,), jnp.float32, least / len(cuts), largest / len(cuts)))
        factor_of = factor_of * jnp.repeat(steps, dims[axis_at] // shards_of).reshape([-1 if axis == axis_at else 1 for axis in range(len(dims))])
    return factor_of


def normal_values(rng, extent, scale, reach, cuts=(), held_as=jnp.bfloat16):
    entries = scale * jax.random.normal(rng, extent, jnp.float32)
    if cuts:
        entries = entries * levels(rng, extent, cuts, -0.22, 0.18)
    return jnp.clip(entries, -reach, reach).astype(held_as)


def setup_inputs(seed: int = 0) -> dict:
    splits = jax.random.split(jax.random.key(seed), 10)
    return {
        "tokens": draw_tokens(jax.random.fold_in(splits[9], 71), 0),
        "cotangent": normal_values(splits[1], (CLIPS_ALL, F, P_SIZE, D), 1.0, 6.0, ((0, 8), (1, 32))),
        "clip_counts": draw_clip_counts(jax.random.fold_in(splits[9], 71), 0),
        "windows": draw_windows(jax.random.fold_in(splits[9], 71), 0),
        "window_counts": draw_window_counts(jax.random.fold_in(splits[9], 71), 0),
        "norm_gain": draw_norm_gain(jax.random.fold_in(splits[9], 71), 0),
        "norm_bias": normal_values(splits[6], (D,), 0.5, 3.0, (), jnp.float32),
        "qkv_weight": draw_qkv_weight(jax.random.fold_in(splits[9], 71), 0),
        "out_weight": normal_values(splits[8], (D, D), D ** -0.5, 0.1875),
    }


EPSILON = 1e-05

def rounded(value):
    return lax.optimization_barrier(value.astype(jnp.bfloat16)).astype(jnp.float32)

def frame_mask(window_list, list_count, frame_count):
    used_slot = jnp.arange(MAXW)[None, :] < list_count[:, None]
    listed = (window_list[:, :, None] == jnp.arange(NWIN)[None, None, :]) & used_slot[:, :, None]
    allowed = jnp.any(listed, axis=1).astype(jnp.float32)
    member = (jnp.arange(frame_count)[:, None] // WIN == jnp.arange(NWIN)[None, :]).astype(jnp.float32)
    return jnp.dot(jnp.dot(member, allowed), member.T) > 0.5

def reference(tokens, cotangent, clip_counts, windows, window_counts, norm_gain, norm_bias, qkv_weight, out_weight):
    slot_index = jnp.arange(CLIPS_ALL)
    live_slot = slot_index % CLIPS < jnp.repeat(clip_counts, CLIPS)
    grad_live = jnp.where(live_slot[:, None, None, None], cotangent, jnp.zeros_like(cotangent))
    qkv_full = qkv_weight.astype(jnp.float32)
    out_full = out_weight.astype(jnp.float32)
    factor = HEAD_DIM ** (-0.5)
    head_shape = (F, P_SIZE, HEADS, HEAD_DIM)

    def clip_step(state_sum, clip_data):
        clip_tokens, clip_grad, window_list, list_count = clip_data
        allowed = frame_mask(window_list, list_count, F)[None, None]
        flat_input = clip_tokens.reshape(F * P_SIZE, D).astype(jnp.float32)
        centred = flat_input - lax.optimization_barrier(jnp.mean(flat_input, axis=1, keepdims=True))
        inv_std = lax.rsqrt(lax.optimization_barrier(jnp.mean(centred * centred, axis=1, keepdims=True)) + EPSILON)
        normal_hat = centred * inv_std
        normed = rounded(normal_hat * norm_gain + norm_bias)
        projected = rounded(jnp.dot(normed, qkv_full))
        query_heads = projected[:, :D].reshape(head_shape)
        key_heads = projected[:, D:2 * D].reshape(head_shape)
        value_heads = projected[:, 2 * D:].reshape(head_shape)
        scores = jnp.einsum('fphd,gphd->phfg', query_heads, key_heads) * factor
        row_max = lax.optimization_barrier(jnp.max(jnp.where(allowed, scores, -1e+30), axis=-1, keepdims=True))
        exp_scores = jnp.where(allowed, jnp.exp(scores - row_max), 0.0)
        attn_prob = exp_scores / lax.optimization_barrier(jnp.sum(exp_scores, axis=-1, keepdims=True))
        prob_bf = rounded(attn_prob)
        attended = rounded(jnp.einsum('phfg,gphd->fphd', prob_bf, value_heads)).reshape(F * P_SIZE, D)
        grad_flat = clip_grad.reshape(F * P_SIZE, D).astype(jnp.float32)
        out_term = jnp.dot(attended.T, grad_flat)
        grad_attn = rounded(jnp.dot(grad_flat, out_full.T)).reshape(head_shape)
        grad_prob = jnp.einsum('fphd,gphd->phfg', grad_attn, value_heads)
        grad_scores = rounded(attn_prob * (grad_prob - lax.optimization_barrier(jnp.sum(attn_prob * grad_prob, axis=-1, keepdims=True))) * factor)
        grad_query = rounded(jnp.einsum('phfg,gphd->fphd', grad_scores, key_heads)).reshape(F * P_SIZE, D)
        grad_keys = rounded(jnp.einsum('phfg,fphd->gphd', grad_scores, query_heads)).reshape(F * P_SIZE, D)
        grad_values = rounded(jnp.einsum('phfg,fphd->gphd', prob_bf, grad_attn)).reshape(F * P_SIZE, D)
        grad_rows = jnp.concatenate([grad_query, grad_keys, grad_values], axis=1)
        grad_normed = jnp.dot(grad_rows, qkv_full.T)
        qkv_term = jnp.dot(normed.T, grad_rows)
        gain_term = lax.optimization_barrier(jnp.sum(grad_normed * normal_hat, axis=0))
        bias_term = lax.optimization_barrier(jnp.sum(grad_normed, axis=0))
        grad_hat = grad_normed * norm_gain
        grad_norm_in = rounded(inv_std * (grad_hat - lax.optimization_barrier(jnp.mean(grad_hat, axis=1, keepdims=True)) - normal_hat * lax.optimization_barrier(jnp.mean(grad_hat * normal_hat, axis=1, keepdims=True))))
        grad_input = (grad_flat + grad_norm_in).astype(jnp.bfloat16).reshape(F, P_SIZE, D)
        new_state = (state_sum[0] + qkv_term, state_sum[1] + out_term, state_sum[2] + gain_term, state_sum[3] + bias_term)
        return (new_state, grad_input)
    initial = (jnp.zeros((D, 3 * D), jnp.float32), jnp.zeros((D, D), jnp.float32), jnp.zeros((D,), jnp.float32), jnp.zeros((D,), jnp.float32))
    final_state, grad_input = lax.scan(clip_step, initial, (tokens, grad_live, windows, window_counts))
    grad_scale = 1.0 / math.sqrt(TOKENS)
    return (grad_input, final_state[0] * grad_scale, final_state[1] * grad_scale, final_state[2] * grad_scale, final_state[3] * grad_scale)
```

```python
from functools import partial
import math

import jax
import jax.numpy as jnp
from jax import lax
from jax.sharding import Mesh, PartitionSpec as P
import numpy as np

D = 1024
HEADS = 16
HEAD_DIM = 64
WIN = 64
MAXW = 3
NWIN = 4


EPSILON = 1e-05


def frame_mask(window_list, list_count, frame_count):
    used_slot = jnp.arange(MAXW)[None, :] < list_count[:, None]
    listed = (window_list[:, :, None] == jnp.arange(NWIN)[None, None, :]) & used_slot[:, :, None]
    allowed = jnp.any(listed, axis=1).astype(jnp.float32)
    member = (jnp.arange(frame_count)[:, None] // WIN == jnp.arange(NWIN)[None, :]).astype(
        jnp.float32
    )
    return jnp.dot(jnp.dot(member, allowed), member.T) > 0.5


def contract_rows(left_side, right_side):
    return lax.dot_general(
        left_side, right_side, (((0,), (0,)), ((), ())), preferred_element_type=jnp.float32
    )


def times_transpose(left_side, right_side):
    return lax.dot_general(
        left_side, right_side, (((1,), (1,)), ((), ())), preferred_element_type=jnp.float32
    )


def local(
    tokens,
    cotangent,
    clip_counts,
    windows,
    window_counts,
    norm_gain,
    norm_bias,
    qkv_weight,
    out_weight,
):
    seq_size = lax.axis_size(("y", "z"))
    rep_size = lax.axis_size(("x", "core"))
    clip_count = tokens.shape[0]
    live_slot = jnp.arange(clip_count) < clip_counts[0]
    grad_live = jnp.where(live_slot[:, None, None, None], cotangent, jnp.zeros_like(cotangent))
    gathered, grad_whole = (
        lax.all_to_all(tokens, ("y", "z"), split_axis=2, concat_axis=1, tiled=True),
        lax.all_to_all(grad_live, ("y", "z"), split_axis=2, concat_axis=1, tiled=True),
    )
    frame_count = gathered.shape[1]
    patch_count = gathered.shape[2]
    row_count = clip_count * frame_count * patch_count
    grad_scale = 1.0 / math.sqrt(clip_count * rep_size * frame_count * patch_count * seq_size)
    factor = HEAD_DIM ** (-0.5)
    head_shape = (clip_count, frame_count, patch_count, HEADS, HEAD_DIM)
    allowed = jax.vmap(partial(frame_mask, frame_count=frame_count))(windows, window_counts)[
        :, None, None
    ]
    flat_input = gathered.reshape(row_count, D).astype(jnp.float32)
    centred = flat_input - jnp.mean(flat_input, axis=1, keepdims=True)
    inv_std = lax.rsqrt(jnp.mean(centred * centred, axis=1, keepdims=True) + EPSILON)
    normal_hat = centred * inv_std
    normed = (normal_hat * norm_gain + norm_bias).astype(jnp.bfloat16)
    projected = jnp.dot(normed, qkv_weight, preferred_element_type=jnp.float32).astype(jnp.bfloat16)
    query_heads = projected[:, :D].reshape(head_shape)
    key_heads = projected[:, D : 2 * D].reshape(head_shape)
    value_heads = projected[:, 2 * D :].reshape(head_shape)
    scores = (
        jnp.einsum("cfphd,cgphd->cphfg", query_heads, key_heads, preferred_element_type=jnp.float32)
        * factor
    )
    row_max = jnp.max(jnp.where(allowed, scores, -1e30), axis=-1, keepdims=True)
    exp_scores = jnp.where(allowed, jnp.exp(scores - row_max), 0.0)
    attn_prob = exp_scores / jnp.sum(exp_scores, axis=-1, keepdims=True)
    prob_bf = attn_prob.astype(jnp.bfloat16)
    attended = jnp.einsum(
        "cphfg,cgphd->cfphd", prob_bf, value_heads, preferred_element_type=jnp.float32
    ).astype(jnp.bfloat16)
    attn_flat = attended.reshape(row_count, D)
    grad_flat = grad_whole.reshape(row_count, D)
    grad_attn = times_transpose(grad_flat, out_weight).astype(jnp.bfloat16).reshape(head_shape)
    grad_prob = jnp.einsum(
        "cfphd,cgphd->cphfg", grad_attn, value_heads, preferred_element_type=jnp.float32
    )
    grad_scores = (
        attn_prob * (grad_prob - jnp.sum(attn_prob * grad_prob, axis=-1, keepdims=True)) * factor
    ).astype(jnp.bfloat16)
    grad_query = jnp.einsum(
        "cphfg,cgphd->cfphd", grad_scores, key_heads, preferred_element_type=jnp.float32
    ).astype(jnp.bfloat16)
    grad_keys = jnp.einsum(
        "cphfg,cfphd->cgphd", grad_scores, query_heads, preferred_element_type=jnp.float32
    ).astype(jnp.bfloat16)
    grad_values = jnp.einsum(
        "cphfg,cfphd->cgphd", prob_bf, grad_attn, preferred_element_type=jnp.float32
    ).astype(jnp.bfloat16)
    grad_rows = jnp.concatenate(
        [
            grad_query.reshape(row_count, D),
            grad_keys.reshape(row_count, D),
            grad_values.reshape(row_count, D),
        ],
        axis=1,
    )
    grad_normed = times_transpose(grad_rows, qkv_weight)
    gain_term = jnp.sum(grad_normed * normal_hat, axis=0) * grad_scale
    bias_term = jnp.sum(grad_normed, axis=0) * grad_scale
    grad_hat = grad_normed * norm_gain
    grad_norm_in = (
        inv_std
        * (
            grad_hat
            - jnp.mean(grad_hat, axis=1, keepdims=True)
            - normal_hat * jnp.mean(grad_hat * normal_hat, axis=1, keepdims=True)
        )
    ).astype(jnp.bfloat16)
    returned = lax.all_to_all(
        grad_norm_in.reshape(clip_count, frame_count, patch_count, D),
        ("y", "z"),
        split_axis=1,
        concat_axis=2,
        tiled=True,
    )
    grad_input = (grad_live.astype(jnp.float32) + returned.astype(jnp.float32)).astype(jnp.bfloat16)
    seq_index = lax.axis_index(("y", "z"))
    side_terms = lax.psum(jnp.stack([gain_term, bias_term]), ("x", "core", "y", "z"))
    side_terms = lax.dynamic_slice_in_dim(side_terms, seq_index * (D // seq_size), D // seq_size, axis=1)
    upper_rows = contract_rows(normed, grad_rows)
    lower_rows = contract_rows(attn_flat, grad_flat)
    stacked = (jnp.concatenate([upper_rows, lower_rows], axis=1) * grad_scale).astype(jnp.bfloat16)
    x_size = lax.axis_size("x")
    width = stacked.shape[1] // (2 * x_size)
    split = stacked.reshape(D, x_size, 2, width)
    core = lax.axis_index("core")
    mine = lax.dynamic_index_in_dim(split, core, axis=2, keepdims=False)
    other = lax.dynamic_index_in_dim(split, 1 - core, axis=2, keepdims=False)
    got = lax.ppermute(other, "core", [(0, 1), (1, 0)])
    merged = (mine.astype(jnp.float32) + got.astype(jnp.float32)).astype(jnp.bfloat16)
    merged = lax.psum_scatter(merged, "y", scatter_dimension=0, tiled=True)
    merged = lax.psum_scatter(merged, "z", scatter_dimension=0, tiled=True)
    merged = lax.psum_scatter(merged, "x", scatter_dimension=1, tiled=True)
    summed = lax.all_gather(
        merged.reshape(merged.shape[0], width), ("x", "core"), axis=1, tiled=True
    ).astype(jnp.float32)
    return (grad_input, summed[:, : 3 * D], summed[:, 3 * D :], side_terms[0], side_terms[1])


def fine_mesh(mesh):
    devices = np.asarray(mesh.devices)
    rep_size, seq_size = devices.shape
    y_size = len({device.coords[1] for device in devices.flat})
    return Mesh(
        devices.reshape(rep_size // 2, 2, y_size, seq_size // y_size), ("x", "core", "y", "z")
    )


def solution(mesh):
    rep, seq = ("x", "core"), ("y", "z")
    return jax.shard_map(
        local,
        mesh=fine_mesh(mesh),
        in_specs=(
            P(rep, seq, None, None),
            P(rep, seq, None, None),
            P(rep),
            P(rep, None, None),
            P(rep, None),
            P(),
            P(),
            P(),
            P(),
        ),
        out_specs=(P(rep, seq, None, None), P(seq, None), P(seq, None), P(seq), P(seq)),
        check_vma=False,
    )
```

```python
from functools import partial
import math

import jax
import jax.numpy as jnp
from jax import lax
from jax.sharding import Mesh, PartitionSpec as P
import numpy as np

D = 1024
HEADS = 16
HEAD_DIM = 64
WIN = 64
MAXW = 3
NWIN = 4


EPSILON = 1e-05


def frame_mask(window_list, list_count, frame_count):
    used_slot = jnp.arange(MAXW)[None, :] < list_count[:, None]
    listed = (window_list[:, :, None] == jnp.arange(NWIN)[None, None, :]) & used_slot[:, :, None]
    allowed = jnp.any(listed, axis=1).astype(jnp.float32)
    member = (jnp.arange(frame_count)[:, None] // WIN == jnp.arange(NWIN)[None, :]).astype(
        jnp.float32
    )
    return jnp.dot(jnp.dot(member, allowed), member.T) > 0.5


def contract_rows(left_side, right_side):
    return lax.dot_general(
        left_side, right_side, (((0,), (0,)), ((), ())), preferred_element_type=jnp.float32
    )


def times_transpose(left_side, right_side):
    return lax.dot_general(
        left_side, right_side, (((1,), (1,)), ((), ())), preferred_element_type=jnp.float32
    )


def local(
    tokens,
    cotangent,
    clip_counts,
    windows,
    window_counts,
    norm_gain,
    norm_bias,
    qkv_weight,
    out_weight,
):
    seq_size = lax.axis_size(("y", "z"))
    rep_size = lax.axis_size(("x", "core"))
    clip_count = tokens.shape[0]
    live_slot = jnp.arange(clip_count) < clip_counts[0]
    grad_live = jnp.where(live_slot[:, None, None, None], cotangent, jnp.zeros_like(cotangent))
    gathered, grad_whole = (
        lax.all_to_all(tokens, ("y", "z"), split_axis=2, concat_axis=1, tiled=True),
        lax.all_to_all(grad_live, ("y", "z"), split_axis=2, concat_axis=1, tiled=True),
    )
    frame_count = gathered.shape[1]
    patch_count = gathered.shape[2]
    row_count = clip_count * frame_count * patch_count
    grad_scale = 1.0 / math.sqrt(clip_count * rep_size * frame_count * patch_count * seq_size)
    factor = HEAD_DIM ** (-0.5)
    head_shape = (clip_count, frame_count, patch_count, HEADS, HEAD_DIM)
    allowed = jax.vmap(partial(frame_mask, frame_count=frame_count))(windows, window_counts)[
        :, None, None
    ]
    flat_input = gathered.reshape(row_count, D).astype(jnp.float32)
    centred = flat_input - jnp.mean(flat_input, axis=1, keepdims=True)
    inv_std = lax.rsqrt(jnp.mean(centred * centred, axis=1, keepdims=True) + EPSILON)
    normal_hat = centred * inv_std
    normed = (normal_hat * norm_gain + norm_bias).astype(jnp.bfloat16)
    projected = jnp.dot(normed, qkv_weight, preferred_element_type=jnp.float32).astype(jnp.bfloat16)
    query_heads = projected[:, :D].reshape(head_shape)
    key_heads = projected[:, D : 2 * D].reshape(head_shape)
    value_heads = projected[:, 2 * D :].reshape(head_shape)
    scores = (
        jnp.einsum("cfphd,cgphd->cphfg", query_heads, key_heads, preferred_element_type=jnp.float32)
        * factor
    )
    row_max = jnp.max(jnp.where(allowed, scores, -1e30), axis=-1, keepdims=True)
    exp_scores = jnp.where(allowed, jnp.exp(scores - row_max), 0.0)
    attn_prob = exp_scores / jnp.sum(exp_scores, axis=-1, keepdims=True)
    prob_bf = attn_prob.astype(jnp.bfloat16)
    attended = jnp.einsum(
        "cphfg,cgphd->cfphd", prob_bf, value_heads, preferred_element_type=jnp.float32
    ).astype(jnp.bfloat16)
    attn_flat = attended.reshape(row_count, D)
    grad_flat = grad_whole.reshape(row_count, D)
    grad_attn = times_transpose(grad_flat, out_weight).astype(jnp.bfloat16).reshape(head_shape)
    grad_prob = jnp.einsum(
        "cfphd,cgphd->cphfg", grad_attn, value_heads, preferred_element_type=jnp.float32
    )
    grad_scores = (
        attn_prob * (grad_prob - jnp.sum(attn_prob * grad_prob, axis=-1, keepdims=True)) * factor
    ).astype(jnp.bfloat16)
    grad_query = jnp.einsum(
        "cphfg,cgphd->cfphd", grad_scores, key_heads, preferred_element_type=jnp.float32
    ).astype(jnp.bfloat16)
    grad_keys = jnp.einsum(
        "cphfg,cfphd->cgphd", grad_scores, query_heads, preferred_element_type=jnp.float32
    ).astype(jnp.bfloat16)
    grad_values = jnp.einsum(
        "cphfg,cfphd->cgphd", prob_bf, grad_attn, preferred_element_type=jnp.float32
    ).astype(jnp.bfloat16)
    grad_rows = jnp.concatenate(
        [
            grad_query.reshape(row_count, D),
            grad_keys.reshape(row_count, D),
            grad_values.reshape(row_count, D),
        ],
        axis=1,
    )
    grad_normed = times_transpose(grad_rows, qkv_weight)
    gain_term = jnp.sum(grad_normed * normal_hat, axis=0) * grad_scale
    bias_term = jnp.sum(grad_normed, axis=0) * grad_scale
    grad_hat = grad_normed * norm_gain
    grad_norm_in = (
        inv_std
        * (
            grad_hat
            - jnp.mean(grad_hat, axis=1, keepdims=True)
            - normal_hat * jnp.mean(grad_hat * normal_hat, axis=1, keepdims=True)
        )
    ).astype(jnp.bfloat16)
    returned = lax.all_to_all(
        grad_norm_in.reshape(clip_count, frame_count, patch_count, D),
        ("y", "z"),
        split_axis=1,
        concat_axis=2,
        tiled=True,
    )
    grad_input = (grad_live.astype(jnp.float32) + returned.astype(jnp.float32)).astype(jnp.bfloat16)
    side_terms = jnp.stack([gain_term, bias_term]).reshape(2, seq_size, D // seq_size)
    side_terms = lax.all_to_all(side_terms, ("y", "z"), split_axis=1, concat_axis=1, tiled=True)
    side_terms = lax.psum(jnp.sum(side_terms, axis=1), ("x", "core"))
    x_size = lax.axis_size("x")
    width = (3 * D + D) // (2 * x_size)
    core = lax.axis_index("core")

    def half_of(index):
        grad_part = lax.dynamic_index_in_dim(
            grad_rows.reshape(row_count, 3 * D // (2 * width), 2, width), index, axis=2, keepdims=False
        ).reshape(row_count, 3 * D // 2)
        flat_part = lax.dynamic_slice_in_dim(grad_flat, index * width, width, axis=1)
        return (
            jnp.concatenate(
                [contract_rows(normed, grad_part), contract_rows(attn_flat, flat_part)], axis=1
            )
            * grad_scale
        ).astype(jnp.bfloat16)

    mine = half_of(core)
    got = lax.ppermute(half_of(1 - core), "core", [(0, 1), (1, 0)])
    merged = (mine.astype(jnp.float32) + got.astype(jnp.float32)).astype(jnp.bfloat16)
    merged = lax.psum_scatter(merged.reshape(D, x_size, width), "y", scatter_dimension=0, tiled=True)
    merged = lax.psum_scatter(merged, "z", scatter_dimension=0, tiled=True)
    merged = lax.psum_scatter(merged, "x", scatter_dimension=1, tiled=True)
    summed = lax.all_gather(
        merged.reshape(merged.shape[0], width), ("x", "core"), axis=1, tiled=True
    ).astype(jnp.float32)
    return (grad_input, summed[:, : 3 * D], summed[:, 3 * D :], side_terms[0], side_terms[1])


def fine_mesh(mesh):
    devices = np.asarray(mesh.devices)
    rep_size, seq_size = devices.shape
    y_size = len({device.coords[1] for device in devices.flat})
    return Mesh(
        devices.reshape(rep_size // 2, 2, y_size, seq_size // y_size), ("x", "core", "y", "z")
    )


def solution(mesh):
    rep, seq = ("x", "core"), ("y", "z")
    return jax.shard_map(
        local,
        mesh=fine_mesh(mesh),
        in_specs=(
            P(rep, seq, None, None),
            P(rep, seq, None, None),
            P(rep),
            P(rep, None, None),
            P(rep, None),
            P(),
            P(),
            P(),
            P(),
        ),
        out_specs=(P(rep, seq, None, None), P(seq, None), P(seq, None), P(seq), P(seq)),
        check_vma=False,
    )
```

```python
from functools import partial
import math

import jax
import jax.numpy as jnp
from jax import lax
from jax.sharding import Mesh, PartitionSpec as P
import numpy as np

D = 1024
HEADS = 16
HEAD_DIM = 64
WIN = 64
MAXW = 3
NWIN = 4


EPSILON = 1e-05


def frame_mask(window_list, list_count, frame_count):
    used_slot = jnp.arange(MAXW)[None, :] < list_count[:, None]
    listed = (window_list[:, :, None] == jnp.arange(NWIN)[None, None, :]) & used_slot[:, :, None]
    allowed = jnp.any(listed, axis=1).astype(jnp.float32)
    member = (jnp.arange(frame_count)[:, None] // WIN == jnp.arange(NWIN)[None, :]).astype(
        jnp.float32
    )
    return jnp.dot(jnp.dot(member, allowed), member.T) > 0.5


def contract_rows(left_side, right_side):
    return lax.dot_general(
        left_side, right_side, (((0,), (0,)), ((), ())), preferred_element_type=jnp.float32
    )


def times_transpose(left_side, right_side):
    return lax.dot_general(
        left_side, right_side, (((1,), (1,)), ((), ())), preferred_element_type=jnp.float32
    )


def local(
    tokens,
    cotangent,
    clip_counts,
    windows,
    window_counts,
    norm_gain,
    norm_bias,
    qkv_weight,
    out_weight,
):
    seq_size = lax.axis_size(("y", "z"))
    rep_size = lax.axis_size(("x", "core"))
    clip_count = tokens.shape[0]
    live_slot = jnp.arange(clip_count) < clip_counts[0]
    grad_live = jnp.where(live_slot[:, None, None, None], cotangent, jnp.zeros_like(cotangent))
    gathered, grad_whole = (
        lax.all_to_all(tokens, ("y", "z"), split_axis=2, concat_axis=1, tiled=True),
        lax.all_to_all(grad_live, ("y", "z"), split_axis=2, concat_axis=1, tiled=True),
    )
    frame_count = gathered.shape[1]
    patch_count = gathered.shape[2]
    row_count = clip_count * frame_count * patch_count
    grad_scale = 1.0 / math.sqrt(clip_count * rep_size * frame_count * patch_count * seq_size)
    factor = HEAD_DIM ** (-0.5)
    head_shape = (clip_count, frame_count, patch_count, HEADS, HEAD_DIM)
    allowed = jax.vmap(partial(frame_mask, frame_count=frame_count))(windows, window_counts)[
        :, None, None
    ]
    flat_input = gathered.reshape(row_count, D).astype(jnp.float32)
    centred = flat_input - jnp.mean(flat_input, axis=1, keepdims=True)
    inv_std = lax.rsqrt(jnp.mean(centred * centred, axis=1, keepdims=True) + EPSILON)
    normal_hat = centred * inv_std
    normed = (normal_hat * norm_gain + norm_bias).astype(jnp.bfloat16)
    normed_rows = normed.reshape(clip_count, frame_count, patch_count, D)
    grad_rows_in = grad_whole.reshape(clip_count, frame_count, patch_count, D)
    projected = jnp.einsum(
        "cfpk,kn->cpnf", normed_rows, qkv_weight, preferred_element_type=jnp.float32
    ).astype(jnp.bfloat16)
    head_shape = (clip_count, patch_count, 3, HEADS, HEAD_DIM, frame_count)
    projected = projected.reshape(head_shape)
    query_heads = projected[:, :, 0]
    key_heads = projected[:, :, 1]
    value_heads = projected[:, :, 2]
    scores = (
        jnp.einsum("cphdf,cphdg->cphfg", query_heads, key_heads, preferred_element_type=jnp.float32)
        * factor
    )
    row_max = jnp.max(jnp.where(allowed, scores, -1e30), axis=-1, keepdims=True)
    exp_scores = jnp.where(allowed, jnp.exp(scores - row_max), 0.0)
    attn_prob = exp_scores / jnp.sum(exp_scores, axis=-1, keepdims=True)
    prob_bf = attn_prob.astype(jnp.bfloat16)
    attended = jnp.einsum(
        "cphfg,cphdg->cphdf", prob_bf, value_heads, preferred_element_type=jnp.float32
    ).astype(jnp.bfloat16)
    grad_flat = grad_whole.reshape(row_count, D)
    grad_attn = (
        jnp.einsum("cfpn,kn->cpkf", grad_rows_in, out_weight, preferred_element_type=jnp.float32)
        .astype(jnp.bfloat16)
        .reshape(clip_count, patch_count, HEADS, HEAD_DIM, frame_count)
    )
    grad_prob = jnp.einsum(
        "cphdf,cphdg->cphfg", grad_attn, value_heads, preferred_element_type=jnp.float32
    )
    grad_scores = (
        attn_prob * (grad_prob - jnp.sum(attn_prob * grad_prob, axis=-1, keepdims=True)) * factor
    ).astype(jnp.bfloat16)
    grad_query = jnp.einsum(
        "cphfg,cphdg->cphdf", grad_scores, key_heads, preferred_element_type=jnp.float32
    ).astype(jnp.bfloat16)
    grad_keys = jnp.einsum(
        "cphfg,cphdf->cphdg", grad_scores, query_heads, preferred_element_type=jnp.float32
    ).astype(jnp.bfloat16)
    grad_values = jnp.einsum(
        "cphfg,cphdf->cphdg", prob_bf, grad_attn, preferred_element_type=jnp.float32
    ).astype(jnp.bfloat16)
    grad_cols = jnp.stack([grad_query, grad_keys, grad_values], axis=2).reshape(
        clip_count, patch_count, 3 * D, frame_count
    )
    grad_normed = jnp.einsum(
        "cpnf,kn->cfpk", grad_cols, qkv_weight, preferred_element_type=jnp.float32
    ).reshape(row_count, D)
    gain_term = jnp.sum(grad_normed * normal_hat, axis=0) * grad_scale
    bias_term = jnp.sum(grad_normed, axis=0) * grad_scale
    grad_hat = grad_normed * norm_gain
    grad_norm_in = (
        inv_std
        * (
            grad_hat
            - jnp.mean(grad_hat, axis=1, keepdims=True)
            - normal_hat * jnp.mean(grad_hat * normal_hat, axis=1, keepdims=True)
        )
    ).astype(jnp.bfloat16)
    returned = lax.all_to_all(
        grad_norm_in.reshape(clip_count, frame_count, patch_count, D),
        ("y", "z"),
        split_axis=1,
        concat_axis=2,
        tiled=True,
    )
    grad_input = (grad_live.astype(jnp.float32) + returned.astype(jnp.float32)).astype(jnp.bfloat16)
    side_terms = jnp.stack([gain_term, bias_term]).reshape(2, seq_size, D // seq_size)
    side_terms = lax.all_to_all(side_terms, ("y", "z"), split_axis=1, concat_axis=1, tiled=True)
    side_terms = lax.psum(jnp.sum(side_terms, axis=1), ("x", "core"))
    x_size = lax.axis_size("x")
    width = (3 * D + D) // (2 * x_size)
    core = lax.axis_index("core")

    attended_cols = attended.reshape(clip_count, patch_count, D, frame_count)

    def half_of(index):
        grad_part = lax.dynamic_index_in_dim(
            grad_cols.reshape(clip_count, patch_count, 3 * D // (2 * width), 2, width, frame_count),
            index,
            axis=3,
            keepdims=False,
        ).reshape(clip_count, patch_count, 3 * D // 2, frame_count)
        flat_part = lax.dynamic_slice_in_dim(grad_rows_in, index * width, width, axis=3)
        upper = jnp.einsum(
            "cfpk,cpnf->kn", normed_rows, grad_part, preferred_element_type=jnp.float32
        )
        lower = jnp.einsum(
            "cpnf,cfpm->nm", attended_cols, flat_part, preferred_element_type=jnp.float32
        )
        return (jnp.concatenate([upper, lower], axis=1) * grad_scale).astype(jnp.bfloat16)

    mine = half_of(core)
    got = lax.ppermute(half_of(1 - core), "core", [(0, 1), (1, 0)])
    merged = (mine.astype(jnp.float32) + got.astype(jnp.float32)).astype(jnp.bfloat16)
    merged = lax.psum_scatter(merged.reshape(D, x_size, width), "y", scatter_dimension=0, tiled=True)
    merged = lax.psum_scatter(merged, "z", scatter_dimension=0, tiled=True)
    merged = lax.psum_scatter(merged, "x", scatter_dimension=1, tiled=True)
    summed = lax.all_gather(
        merged.reshape(merged.shape[0], width), ("x", "core"), axis=1, tiled=True
    ).astype(jnp.float32)
    return (grad_input, summed[:, : 3 * D], summed[:, 3 * D :], side_terms[0], side_terms[1])


def fine_mesh(mesh):
    devices = np.asarray(mesh.devices)
    rep_size, seq_size = devices.shape
    y_size = len({device.coords[1] for device in devices.flat})
    return Mesh(
        devices.reshape(rep_size // 2, 2, y_size, seq_size // y_size), ("x", "core", "y", "z")
    )


def solution(mesh):
    rep, seq = ("x", "core"), ("y", "z")
    return jax.shard_map(
        local,
        mesh=fine_mesh(mesh),
        in_specs=(
            P(rep, seq, None, None),
            P(rep, seq, None, None),
            P(rep),
            P(rep, None, None),
            P(rep, None),
            P(),
            P(),
            P(),
            P(),
        ),
        out_specs=(P(rep, seq, None, None), P(seq, None), P(seq, None), P(seq), P(seq)),
        check_vma=False,
    )
```

```python
from functools import partial
import math

import jax
import jax.numpy as jnp
from jax import lax
from jax.sharding import Mesh, PartitionSpec as P
import numpy as np

D = 1024
HEADS = 16
HEAD_DIM = 64
WIN = 64
MAXW = 3
NWIN = 4


EPSILON = 1e-05


def frame_mask(window_list, list_count, frame_count):
    used_slot = jnp.arange(MAXW)[None, :] < list_count[:, None]
    listed = (window_list[:, :, None] == jnp.arange(NWIN)[None, None, :]) & used_slot[:, :, None]
    allowed = jnp.any(listed, axis=1).astype(jnp.float32)
    member = (jnp.arange(frame_count)[:, None] // WIN == jnp.arange(NWIN)[None, :]).astype(
        jnp.float32
    )
    return jnp.dot(jnp.dot(member, allowed), member.T) > 0.5


def local(
    tokens,
    cotangent,
    clip_counts,
    windows,
    window_counts,
    norm_gain,
    norm_bias,
    qkv_weight,
    out_weight,
):
    seq_size = lax.axis_size(("y", "z"))
    rep_size = lax.axis_size(("x", "core"))
    clip_count = tokens.shape[0]
    live_slot = jnp.arange(clip_count) < clip_counts[0]
    grad_live = jnp.where(live_slot[:, None, None, None], cotangent, jnp.zeros_like(cotangent))
    gathered = lax.all_to_all(tokens, ("y", "z"), split_axis=2, concat_axis=1, tiled=True)
    grad_whole = lax.all_to_all(grad_live, ("y", "z"), split_axis=2, concat_axis=1, tiled=True)
    frame_count = gathered.shape[1]
    patch_count = gathered.shape[2]
    row_count = clip_count * frame_count * patch_count
    grad_scale = 1.0 / math.sqrt(clip_count * rep_size * frame_count * patch_count * seq_size)
    factor = HEAD_DIM ** (-0.5)
    head_shape = (clip_count, frame_count, patch_count, HEADS, HEAD_DIM)
    allowed = jax.vmap(partial(frame_mask, frame_count=frame_count))(windows, window_counts)[
        :, None, None
    ]
    flat_input = gathered.reshape(row_count, D).astype(jnp.float32)
    centred = flat_input - jnp.mean(flat_input, axis=1, keepdims=True)
    inv_std = lax.rsqrt(jnp.mean(centred * centred, axis=1, keepdims=True) + EPSILON)
    normal_hat = centred * inv_std
    normed = (normal_hat * norm_gain + norm_bias).astype(jnp.bfloat16)
    normed_rows = normed.reshape(clip_count, frame_count, patch_count, D)
    grad_rows_in = grad_whole.reshape(clip_count, frame_count, patch_count, D)
    projected = jnp.einsum(
        "cfpk,kn->cpnf", normed_rows, qkv_weight, preferred_element_type=jnp.float32
    ).astype(jnp.bfloat16)
    head_shape = (clip_count, patch_count, 3, HEADS, HEAD_DIM, frame_count)
    projected = projected.reshape(head_shape)
    query_heads = projected[:, :, 0]
    key_heads = projected[:, :, 1]
    value_heads = projected[:, :, 2]
    scores = (
        jnp.einsum("cphdf,cphdg->cphfg", query_heads, key_heads, preferred_element_type=jnp.float32)
        * factor
    )
    row_max = jnp.max(jnp.where(allowed, scores, -1e30), axis=-1, keepdims=True)
    exp_scores = jnp.where(allowed, jnp.exp(scores - row_max), 0.0)
    attn_prob = exp_scores / jnp.sum(exp_scores, axis=-1, keepdims=True)
    prob_bf = attn_prob.astype(jnp.bfloat16)
    attended = jnp.einsum(
        "cphfg,cphdg->cphdf", prob_bf, value_heads, preferred_element_type=jnp.float32
    ).astype(jnp.bfloat16)
    grad_attn = (
        jnp.einsum("cfpn,kn->cpkf", grad_rows_in, out_weight, preferred_element_type=jnp.float32)
        .astype(jnp.bfloat16)
        .reshape(clip_count, patch_count, HEADS, HEAD_DIM, frame_count)
    )
    grad_prob = jnp.einsum(
        "cphdf,cphdg->cphfg", grad_attn, value_heads, preferred_element_type=jnp.float32
    )
    grad_scores = (
        attn_prob * (grad_prob - jnp.sum(attn_prob * grad_prob, axis=-1, keepdims=True)) * factor
    ).astype(jnp.bfloat16)
    grad_query = jnp.einsum(
        "cphfg,cphdg->cphdf", grad_scores, key_heads, preferred_element_type=jnp.float32
    ).astype(jnp.bfloat16)
    grad_keys = jnp.einsum(
        "cphfg,cphdf->cphdg", grad_scores, query_heads, preferred_element_type=jnp.float32
    ).astype(jnp.bfloat16)
    grad_values = jnp.einsum(
        "cphfg,cphdf->cphdg", prob_bf, grad_attn, preferred_element_type=jnp.float32
    ).astype(jnp.bfloat16)
    grad_cols = jnp.stack([grad_query, grad_keys, grad_values], axis=2).reshape(
        clip_count, patch_count, 3 * D, frame_count
    )
    grad_normed = jnp.einsum(
        "cpnf,kn->cfpk", grad_cols, qkv_weight, preferred_element_type=jnp.float32
    ).reshape(row_count, D)
    gain_term = jnp.sum(grad_normed * normal_hat, axis=0) * grad_scale
    bias_term = jnp.sum(grad_normed, axis=0) * grad_scale
    grad_hat = grad_normed * norm_gain
    grad_norm_in = (
        inv_std
        * (
            grad_hat
            - jnp.mean(grad_hat, axis=1, keepdims=True)
            - normal_hat * jnp.mean(grad_hat * normal_hat, axis=1, keepdims=True)
        )
    ).astype(jnp.bfloat16)
    returned = lax.all_to_all(
        grad_norm_in.reshape(clip_count, frame_count, patch_count, D),
        ("y", "z"),
        split_axis=1,
        concat_axis=2,
        tiled=True,
    )
    grad_input = (grad_live.astype(jnp.float32) + returned.astype(jnp.float32)).astype(jnp.bfloat16)
    side_terms = jnp.stack([gain_term, bias_term]).reshape(2, seq_size, D // seq_size)
    side_terms = lax.all_to_all(side_terms, ("y", "z"), split_axis=1, concat_axis=1, tiled=True)
    side_terms = lax.psum(jnp.sum(side_terms, axis=1), ("x", "core"))
    x_size = lax.axis_size("x")
    width = (3 * D + D) // (2 * x_size)
    core = lax.axis_index("core")

    attended_cols = attended.reshape(clip_count, patch_count, D, frame_count)

    def half_of(index):
        grad_part = lax.dynamic_index_in_dim(
            grad_cols.reshape(clip_count, patch_count, 3 * D // (2 * width), 2, width, frame_count),
            index,
            axis=3,
            keepdims=False,
        ).reshape(clip_count, patch_count, 3 * D // 2, frame_count)
        flat_part = lax.dynamic_slice_in_dim(grad_rows_in, index * width, width, axis=3)
        upper = jnp.einsum(
            "cfpk,cpnf->kn", normed_rows, grad_part, preferred_element_type=jnp.float32
        )
        lower = jnp.einsum(
            "cpnf,cfpm->nm", attended_cols, flat_part, preferred_element_type=jnp.float32
        )
        return (jnp.concatenate([upper, lower], axis=1) * grad_scale).astype(jnp.bfloat16)

    mine = half_of(core)
    got = lax.ppermute(half_of(1 - core), "core", [(0, 1), (1, 0)])
    merged = (mine.astype(jnp.float32) + got.astype(jnp.float32)).astype(jnp.bfloat16)
    merged = lax.psum_scatter(merged.reshape(D, x_size, width), "y", scatter_dimension=0, tiled=True)
    z_size = lax.axis_size("z")
    z_index = lax.axis_index("z")
    blocks = merged.reshape(z_size, merged.shape[0] // z_size, *merged.shape[1:])
    total = lax.dynamic_index_in_dim(blocks, z_index, axis=0, keepdims=False).astype(jnp.float32)
    for shift in range(1, z_size):
        outgoing = lax.dynamic_index_in_dim(blocks, (z_index + shift) % z_size, axis=0, keepdims=False)
        pairs = [(source, (source + shift) % z_size) for source in range(z_size)]
        total = total + lax.ppermute(outgoing, "z", pairs).astype(jnp.float32)
    merged = total.astype(jnp.bfloat16)
    merged = lax.psum_scatter(merged, "x", scatter_dimension=1, tiled=True)
    summed = lax.all_gather(
        merged.reshape(merged.shape[0], width), ("x", "core"), axis=1, tiled=True
    ).astype(jnp.float32)
    return (grad_input, summed[:, : 3 * D], summed[:, 3 * D :], side_terms[0], side_terms[1])


def fine_mesh(mesh):
    devices = np.asarray(mesh.devices)
    rep_size, seq_size = devices.shape
    y_size = len({device.coords[1] for device in devices.flat})
    return Mesh(
        devices.reshape(rep_size // 2, 2, y_size, seq_size // y_size), ("x", "core", "y", "z")
    )


def solution(mesh):
    rep, seq = ("x", "core"), ("y", "z")
    fine = fine_mesh(mesh)
    return jax.shard_map(
        local,
        mesh=fine,
        in_specs=(
            P(rep, seq, None, None),
            P(rep, seq, None, None),
            P(rep),
            P(rep, None, None),
            P(rep, None),
            P(),
            P(),
            P(),
            P(),
        ),
        out_specs=(P(rep, seq, None, None), P(seq, None), P(seq, None), P(seq), P(seq)),
        check_vma=False,
    )
```

```python
from functools import partial
import math

import jax
import jax.numpy as jnp
from jax import lax
from jax.sharding import Mesh, PartitionSpec as P
import numpy as np

D = 1024
HEADS = 16
HEAD_DIM = 64
WIN = 64
MAXW = 3
NWIN = 4


EPSILON = 1e-05


def frame_mask(window_list, list_count, frame_count):
    used_slot = jnp.arange(MAXW)[None, :] < list_count[:, None]
    listed = (window_list[:, :, None] == jnp.arange(NWIN)[None, None, :]) & used_slot[:, :, None]
    allowed = jnp.any(listed, axis=1).astype(jnp.float32)
    member = (jnp.arange(frame_count)[:, None] // WIN == jnp.arange(NWIN)[None, :]).astype(
        jnp.float32
    )
    return jnp.dot(jnp.dot(member, allowed), member.T) > 0.5


def local(
    tokens,
    cotangent,
    clip_counts,
    windows,
    window_counts,
    norm_gain,
    norm_bias,
    qkv_weight,
    out_weight,
):
    seq_size = lax.axis_size(("y", "z"))
    rep_size = lax.axis_size(("x", "core"))
    clip_count = tokens.shape[0]
    live_slot = jnp.arange(clip_count) < clip_counts[0]
    grad_live = jnp.where(live_slot[:, None, None, None], cotangent, jnp.zeros_like(cotangent))
    gathered = lax.all_to_all(tokens, ("y", "z"), split_axis=2, concat_axis=1, tiled=True)
    grad_whole = lax.all_to_all(grad_live, ("y", "z"), split_axis=2, concat_axis=1, tiled=True)
    frame_count = gathered.shape[1]
    patch_count = gathered.shape[2]
    row_count = clip_count * frame_count * patch_count
    grad_scale = 1.0 / math.sqrt(clip_count * rep_size * frame_count * patch_count * seq_size)
    factor = HEAD_DIM ** (-0.5)
    head_shape = (clip_count, frame_count, patch_count, HEADS, HEAD_DIM)
    allowed = jax.vmap(partial(frame_mask, frame_count=frame_count))(windows, window_counts)[
        :, None, None
    ]
    flat_input = gathered.reshape(row_count, D).astype(jnp.float32)
    centred = flat_input - jnp.mean(flat_input, axis=1, keepdims=True)
    inv_std = lax.rsqrt(jnp.mean(centred * centred, axis=1, keepdims=True) + EPSILON)
    normal_hat = centred * inv_std
    normed = (normal_hat * norm_gain + norm_bias).astype(jnp.bfloat16)
    normed_rows = normed.reshape(clip_count, frame_count, patch_count, D)
    grad_rows_in = grad_whole.reshape(clip_count, frame_count, patch_count, D)
    projected = jnp.einsum(
        "cfpk,kn->cpnf", normed_rows, qkv_weight, preferred_element_type=jnp.float32
    ).astype(jnp.bfloat16)
    head_shape = (clip_count, patch_count, 3, HEADS, HEAD_DIM, frame_count)
    projected = projected.reshape(head_shape)
    query_heads = projected[:, :, 0]
    key_heads = projected[:, :, 1]
    value_heads = projected[:, :, 2]
    scores = (
        jnp.einsum("cphdf,cphdg->cphfg", query_heads, key_heads, preferred_element_type=jnp.float32)
        * factor
    )
    row_max = jnp.max(jnp.where(allowed, scores, -1e30), axis=-1, keepdims=True)
    exp_scores = jnp.where(allowed, jnp.exp(scores - row_max), 0.0)
    attn_prob = exp_scores / jnp.sum(exp_scores, axis=-1, keepdims=True)
    prob_bf = attn_prob.astype(jnp.bfloat16)
    attended = jnp.einsum(
        "cphfg,cphdg->cphdf", prob_bf, value_heads, preferred_element_type=jnp.float32
    ).astype(jnp.bfloat16)
    grad_attn = (
        jnp.einsum("cfpn,kn->cpkf", grad_rows_in, out_weight, preferred_element_type=jnp.float32)
        .astype(jnp.bfloat16)
        .reshape(clip_count, patch_count, HEADS, HEAD_DIM, frame_count)
    )
    grad_prob = jnp.einsum(
        "cphdf,cphdg->cphfg", grad_attn, value_heads, preferred_element_type=jnp.float32
    )
    grad_scores = (
        attn_prob * (grad_prob - jnp.sum(attn_prob * grad_prob, axis=-1, keepdims=True)) * factor
    ).astype(jnp.bfloat16)
    grad_scores = lax.optimization_barrier(grad_scores)
    grad_query = jnp.einsum(
        "cphfg,cphdg->cphdf", grad_scores, key_heads, preferred_element_type=jnp.float32
    ).astype(jnp.bfloat16)
    grad_keys = jnp.einsum(
        "cphfg,cphdf->cphdg", grad_scores, query_heads, preferred_element_type=jnp.float32
    ).astype(jnp.bfloat16)
    grad_values = jnp.einsum(
        "cphfg,cphdf->cphdg", prob_bf, grad_attn, preferred_element_type=jnp.float32
    ).astype(jnp.bfloat16)
    grad_cols = jnp.stack([grad_query, grad_keys, grad_values], axis=2).reshape(
        clip_count, patch_count, 3 * D, frame_count
    )
    grad_normed = jnp.einsum(
        "cpnf,kn->cfpk", grad_cols, qkv_weight, preferred_element_type=jnp.float32
    ).reshape(row_count, D)
    gain_term = jnp.sum(grad_normed * normal_hat, axis=0) * grad_scale
    bias_term = jnp.sum(grad_normed, axis=0) * grad_scale
    grad_hat = grad_normed * norm_gain
    grad_norm_in = (
        inv_std
        * (
            grad_hat
            - jnp.mean(grad_hat, axis=1, keepdims=True)
            - normal_hat * jnp.mean(grad_hat * normal_hat, axis=1, keepdims=True)
        )
    ).astype(jnp.bfloat16)
    returned = lax.all_to_all(
        grad_norm_in.reshape(clip_count, frame_count, patch_count, D),
        ("y", "z"),
        split_axis=1,
        concat_axis=2,
        tiled=True,
    )
    grad_input = (grad_live.astype(jnp.float32) + returned.astype(jnp.float32)).astype(jnp.bfloat16)
    side_terms = jnp.stack([gain_term, bias_term]).reshape(2, seq_size, D // seq_size)
    side_terms = lax.all_to_all(side_terms, ("y", "z"), split_axis=1, concat_axis=1, tiled=True)
    side_terms = lax.psum(jnp.sum(side_terms, axis=1), ("x", "core"))
    x_size = lax.axis_size("x")
    width = (3 * D + D) // (2 * x_size)
    core = lax.axis_index("core")

    attended_cols = attended.reshape(clip_count, patch_count, D, frame_count)

    def half_of(index):
        grad_part = lax.dynamic_index_in_dim(
            grad_cols.reshape(clip_count, patch_count, 3 * D // (2 * width), 2, width, frame_count),
            index,
            axis=3,
            keepdims=False,
        ).reshape(clip_count, patch_count, 3 * D // 2, frame_count)
        flat_part = lax.dynamic_slice_in_dim(grad_rows_in, index * width, width, axis=3)
        upper = jnp.einsum(
            "cfpk,cpnf->kn", normed_rows, grad_part, preferred_element_type=jnp.float32
        )
        lower = jnp.einsum(
            "cpnf,cfpm->nm", attended_cols, flat_part, preferred_element_type=jnp.float32
        )
        return (jnp.concatenate([upper, lower], axis=1) * grad_scale).astype(jnp.bfloat16)

    mine = half_of(core)
    got = lax.ppermute(half_of(1 - core), "core", [(0, 1), (1, 0)])
    merged = (mine.astype(jnp.float32) + got.astype(jnp.float32)).astype(jnp.bfloat16)
    merged = lax.psum_scatter(merged.reshape(D, x_size, width), "y", scatter_dimension=0, tiled=True)
    merged = lax.psum_scatter(merged, "z", scatter_dimension=0, tiled=True)
    merged = lax.psum_scatter(merged, "x", scatter_dimension=1, tiled=True)
    summed = lax.all_gather(
        merged.reshape(merged.shape[0], width), ("x", "core"), axis=1, tiled=True
    ).astype(jnp.float32)
    return (grad_input, summed[:, : 3 * D], summed[:, 3 * D :], side_terms[0], side_terms[1])


def fine_mesh(mesh):
    devices = np.asarray(mesh.devices)
    rep_size, seq_size = devices.shape
    y_size = len({device.coords[1] for device in devices.flat})
    return Mesh(
        devices.reshape(rep_size // 2, 2, y_size, seq_size // y_size), ("x", "core", "y", "z")
    )


def solution(mesh):
    rep, seq = ("x", "core"), ("y", "z")
    fine = fine_mesh(mesh)
    return jax.shard_map(
        local,
        mesh=fine,
        in_specs=(
            P(rep, seq, None, None),
            P(rep, seq, None, None),
            P(rep),
            P(rep, None, None),
            P(rep, None),
            P(),
            P(),
            P(),
            P(),
        ),
        out_specs=(P(rep, seq, None, None), P(seq, None), P(seq, None), P(seq), P(seq)),
        check_vma=False,
    )
```

```python
from functools import partial
import math

import jax
import jax.numpy as jnp
from jax import lax
from jax.sharding import Mesh, PartitionSpec as P
import numpy as np

D = 1024
HEADS = 16
HEAD_DIM = 64
WIN = 64
MAXW = 3
NWIN = 4


EPSILON = 1e-05


def frame_mask(window_list, list_count, frame_count):
    used_slot = jnp.arange(MAXW)[None, :] < list_count[:, None]
    listed = (window_list[:, :, None] == jnp.arange(NWIN)[None, None, :]) & used_slot[:, :, None]
    allowed = jnp.any(listed, axis=1).astype(jnp.float32)
    member = (jnp.arange(frame_count)[:, None] // WIN == jnp.arange(NWIN)[None, :]).astype(
        jnp.float32
    )
    return jnp.dot(jnp.dot(member, allowed), member.T) > 0.5


def local(
    tokens,
    cotangent,
    clip_counts,
    windows,
    window_counts,
    norm_gain,
    norm_bias,
    qkv_weight,
    out_weight,
):
    seq_size = lax.axis_size(("y", "z"))
    rep_size = lax.axis_size(("x", "core"))
    clip_count = tokens.shape[0]
    live_slot = jnp.arange(clip_count) < clip_counts[0]
    grad_live = jnp.where(live_slot[:, None, None, None], cotangent, jnp.zeros_like(cotangent))
    gathered = lax.all_to_all(tokens, ("y", "z"), split_axis=2, concat_axis=1, tiled=True)
    grad_whole = lax.all_to_all(grad_live, ("y", "z"), split_axis=2, concat_axis=1, tiled=True)
    frame_count = gathered.shape[1]
    patch_count = gathered.shape[2]
    row_count = clip_count * frame_count * patch_count
    grad_scale = 1.0 / math.sqrt(clip_count * rep_size * frame_count * patch_count * seq_size)
    factor = HEAD_DIM ** (-0.5)
    head_shape = (clip_count, frame_count, patch_count, HEADS, HEAD_DIM)
    allowed = jax.vmap(partial(frame_mask, frame_count=frame_count))(windows, window_counts)[
        :, None, None
    ]
    flat_input = gathered.reshape(row_count, D).astype(jnp.float32)
    centred = flat_input - jnp.mean(flat_input, axis=1, keepdims=True)
    inv_std = lax.rsqrt(jnp.mean(centred * centred, axis=1, keepdims=True) + EPSILON)
    normal_hat = centred * inv_std
    normed = (normal_hat * norm_gain + norm_bias).astype(jnp.bfloat16)
    normed_rows = normed.reshape(clip_count, frame_count, patch_count, D)
    grad_rows_in = grad_whole.reshape(clip_count, frame_count, patch_count, D)
    projected = jnp.einsum(
        "cfpk,kn->cpnf", normed_rows, qkv_weight, preferred_element_type=jnp.float32
    ).astype(jnp.bfloat16)
    head_shape = (clip_count, patch_count, 3, HEADS, HEAD_DIM, frame_count)
    projected = projected.reshape(head_shape)
    query_heads = projected[:, :, 0]
    key_heads = projected[:, :, 1]
    value_heads = projected[:, :, 2]
    scores = (
        jnp.einsum("cphdf,cphdg->cphfg", query_heads, key_heads, preferred_element_type=jnp.float32)
        * factor
    )
    row_max = jnp.max(jnp.where(allowed, scores, -1e30), axis=-1, keepdims=True)
    exp_scores = jnp.where(allowed, jnp.exp(scores - row_max), 0.0)
    attn_prob = exp_scores / jnp.sum(exp_scores, axis=-1, keepdims=True)
    prob_bf = attn_prob.astype(jnp.bfloat16)
    attended = jnp.einsum(
        "cphfg,cphdg->cphdf", prob_bf, value_heads, preferred_element_type=jnp.float32
    ).astype(jnp.bfloat16)
    grad_attn = (
        jnp.einsum("cfpn,kn->cpkf", grad_rows_in, out_weight, preferred_element_type=jnp.float32)
        .astype(jnp.bfloat16)
        .reshape(clip_count, patch_count, HEADS, HEAD_DIM, frame_count)
    )
    grad_prob = jnp.einsum(
        "cphdf,cphdg->cphfg", grad_attn, value_heads, preferred_element_type=jnp.float32
    )
    grad_scores = (
        attn_prob * (grad_prob - jnp.sum(attn_prob * grad_prob, axis=-1, keepdims=True)) * factor
    ).astype(jnp.bfloat16)
    grad_scores, grad_scores_t = lax.optimization_barrier(
        (grad_scores, jnp.swapaxes(grad_scores, -1, -2))
    )
    grad_query = jnp.einsum(
        "cphfg,cphdg->cphdf", grad_scores, key_heads, preferred_element_type=jnp.float32
    ).astype(jnp.bfloat16)
    grad_keys = jnp.einsum(
        "cphgf,cphdf->cphdg", grad_scores_t, query_heads, preferred_element_type=jnp.float32
    ).astype(jnp.bfloat16)
    grad_values = jnp.einsum(
        "cphfg,cphdf->cphdg", prob_bf, grad_attn, preferred_element_type=jnp.float32
    ).astype(jnp.bfloat16)
    grad_cols = jnp.stack([grad_query, grad_keys, grad_values], axis=2).reshape(
        clip_count, patch_count, 3 * D, frame_count
    )
    grad_normed = jnp.einsum(
        "cpnf,kn->cfpk", grad_cols, qkv_weight, preferred_element_type=jnp.float32
    ).reshape(row_count, D)
    gain_term = jnp.sum(grad_normed * normal_hat, axis=0) * grad_scale
    bias_term = jnp.sum(grad_normed, axis=0) * grad_scale
    grad_hat = grad_normed * norm_gain
    grad_norm_in = (
        inv_std
        * (
            grad_hat
            - jnp.mean(grad_hat, axis=1, keepdims=True)
            - normal_hat * jnp.mean(grad_hat * normal_hat, axis=1, keepdims=True)
        )
    ).astype(jnp.bfloat16)
    returned = lax.all_to_all(
        grad_norm_in.reshape(clip_count, frame_count, patch_count, D),
        ("y", "z"),
        split_axis=1,
        concat_axis=2,
        tiled=True,
    )
    grad_input = (grad_live.astype(jnp.float32) + returned.astype(jnp.float32)).astype(jnp.bfloat16)
    side_terms = jnp.stack([gain_term, bias_term]).reshape(2, seq_size, D // seq_size)
    side_terms = lax.all_to_all(side_terms, ("y", "z"), split_axis=1, concat_axis=1, tiled=True)
    side_terms = lax.psum(jnp.sum(side_terms, axis=1), ("x", "core"))
    x_size = lax.axis_size("x")
    width = (3 * D + D) // (2 * x_size)
    core = lax.axis_index("core")

    attended_cols = attended.reshape(clip_count, patch_count, D, frame_count)

    def half_of(index):
        grad_part = lax.dynamic_index_in_dim(
            grad_cols.reshape(clip_count, patch_count, 3 * D // (2 * width), 2, width, frame_count),
            index,
            axis=3,
            keepdims=False,
        ).reshape(clip_count, patch_count, 3 * D // 2, frame_count)
        flat_part = lax.dynamic_slice_in_dim(grad_rows_in, index * width, width, axis=3)
        upper = jnp.einsum(
            "cfpk,cpnf->kn", normed_rows, grad_part, preferred_element_type=jnp.float32
        )
        lower = jnp.einsum(
            "cpnf,cfpm->nm", attended_cols, flat_part, preferred_element_type=jnp.float32
        )
        return (jnp.concatenate([upper, lower], axis=1) * grad_scale).astype(jnp.bfloat16)

    mine = half_of(core)
    got = lax.ppermute(half_of(1 - core), "core", [(0, 1), (1, 0)])
    merged = (mine.astype(jnp.float32) + got.astype(jnp.float32)).astype(jnp.bfloat16)
    merged = lax.psum_scatter(merged.reshape(D, x_size, width), "y", scatter_dimension=0, tiled=True)
    merged = lax.psum_scatter(merged, "z", scatter_dimension=0, tiled=True)
    merged = lax.psum_scatter(merged, "x", scatter_dimension=1, tiled=True)
    summed = lax.all_gather(
        merged.reshape(merged.shape[0], width), ("x", "core"), axis=1, tiled=True
    ).astype(jnp.float32)
    return (grad_input, summed[:, : 3 * D], summed[:, 3 * D :], side_terms[0], side_terms[1])


def fine_mesh(mesh):
    devices = np.asarray(mesh.devices)
    rep_size, seq_size = devices.shape
    y_size = len({device.coords[1] for device in devices.flat})
    return Mesh(
        devices.reshape(rep_size // 2, 2, y_size, seq_size // y_size), ("x", "core", "y", "z")
    )


def solution(mesh):
    rep, seq = ("x", "core"), ("y", "z")
    fine = fine_mesh(mesh)
    return jax.shard_map(
        local,
        mesh=fine,
        in_specs=(
            P(rep, seq, None, None),
            P(rep, seq, None, None),
            P(rep),
            P(rep, None, None),
            P(rep, None),
            P(),
            P(),
            P(),
            P(),
        ),
        out_specs=(P(rep, seq, None, None), P(seq, None), P(seq, None), P(seq), P(seq)),
        check_vma=False,
    )
```
